768 devices in a mesh: occ: 128 (over x, z_lo, y), aux: 6 (over z_hi, core).
Axes of the slice: x: 4, y: 8, z: 12 (z_hi: 3, z_lo: 4; z = z_hi * 4 + z_lo), core: 2. Of those that a mesh axis runs over, the one named last changes fastest.
Arguments:
- b_rows: bfloat16 [12288, 16384], P('aux', 'occ'), may hold values from -0.5 to 0.5
- b_cols: bfloat16 [12288, 65536], P('aux', 'occ'), may hold values from -0.5 to 0.5
- eps_occ: float32 [256], replicated, may hold values from -1.5 to -0.3
- eps_va: float32 [64], replicated, may hold values from 0.2 to 2
- eps_vb: float32 [256], replicated, may hold values from 0.2 to 2
Outputs:
- gamma: float32 [12288, 16384], P('aux', 'occ')
The draws below stay inside these ranges and needn't reach their ends.
All inputs are finite; a program needn't handle non-finite values.
Results may differ from the reference program's by a relative error of at most 0.0027.
Values may be sent and summed in bfloat16 or wider, within the bound.
No kernel may reach another device: no remote copies, remote signals or barrier semaphores. Data moves between devices by JAX's collectives and lax.ppermute only.
A program may use at most 32 MiB of HBM per device.

```python
import jax
import jax.numpy as jnp
from jax import lax

NAUX = 12288
VA = 64
VB = 256
OCC_DEV = 2
NOCC = 256
N_OCC = 128


def levels(own_key, dims, shards, least, high):
    def one(axis_at, parts):
        steps = jax.random.uniform(jax.random.fold_in(jax.random.fold_in(own_key, 6), axis_at), (parts,), jnp.float32, least / len(shards), high / len(shards))
        return jnp.repeat(jnp.exp(steps), dims[axis_at] // parts).reshape((-1,) + (1,) * (len(dims) - axis_at - 1))

    factor_of = one(*shards[0])
    for cut in shards[1:]:
        factor_of = factor_of * one(*cut)
    return factor_of


def centred(stream_key, dims, spread, bound, split=(), kind=jnp.bfloat16):
    entries = jax.random.normal(stream_key, dims, jnp.float32) * spread
    if len(split) > 0:
        entries = levels(stream_key, dims, split, -0.22, 0.18) * entries
    return jnp.clip(entries, min=-bound, max=bound).astype(kind)


def setup_inputs(seed: int = 0) -> dict:
    key_list = jax.random.split(jax.random.key(seed), 6)
    return {
        "b_rows": centred(key_list[0], (NAUX, NOCC * VA), 0.08, 0.5, ((0, 6), (1, 128))),
        "b_cols": centred(key_list[1], (NAUX, NOCC * VB), 0.08, 0.5, ((0, 6), (1, 128))),
        "eps_occ": jnp.clip(jax.random.uniform(key_list[2], (NOCC,), jnp.float32, -1.5, -0.3), -1.5, -0.3),
        "eps_va": jnp.clip(jax.random.uniform(key_list[3], (VA,), jnp.float32, 0.2, 2.0), 0.2, 2.0),
        "eps_vb": jnp.clip(jax.random.uniform(key_list[4], (VB,), jnp.float32, 0.2, 2.0), 0.2, 2.0),
    }


spin_scale = 1.3


def energy_row(eps_occ, virt_energy, which, per_block):
    occ_energy = lax.dynamic_slice_in_dim(eps_occ, which * per_block, per_block)
    return (virt_energy[None, :] - occ_energy[:, None]).reshape(-1)


def reference(b_rows, b_cols, eps_occ, eps_va, eps_vb):
    width_rows = OCC_DEV * VA
    width_cols = OCC_DEV * VB

    def one_block(which):
        left_block = lax.dynamic_slice_in_dim(b_rows, which * width_rows, width_rows, 1)
        row_energy = energy_row(eps_occ, eps_va, which, OCC_DEV)
        total = jnp.zeros((NAUX, width_rows), jnp.float32)
        for shift_index in range(3):
            partner = ((which - shift_index) % N_OCC).astype(jnp.int32)
            right_block = lax.dynamic_slice_in_dim(b_cols, partner * width_cols, width_cols, 1)
            col_energy = energy_row(eps_occ, eps_vb, partner, OCC_DEV)
            summed = lax.dot_general(left_block, right_block, (((0,), (0,)), ((), ())), preferred_element_type=jnp.float32)
            amplitude = (spin_scale * summed / (row_energy[:, None] + col_energy[None, :])).astype(jnp.bfloat16)
            total = total + lax.dot_general(right_block, amplitude, (((1,), (1,)), ((), ())), preferred_element_type=jnp.float32)
        return total

    blocks = lax.map(one_block, jnp.arange(N_OCC, dtype=jnp.int32))
    return jnp.transpose(blocks, (1, 0, 2)).reshape(NAUX, N_OCC * width_rows)
```

```python
import jax
import jax.numpy as jnp
from jax import lax
from jax.sharding import PartitionSpec as P

spin_scale = 1.3


def shifted(value, axis, by):
    size = lax.axis_size(axis)
    return lax.ppermute(value, axis, [(i, (i + by) % size) for i in range(size)])


def aux_pairs(size, step_core, step_chip):
    pairs = []
    for i in range(size):
        chip, core = divmod(i, 2)
        chips = size // 2
        pairs.append((i, ((chip + step_chip) % chips) * 2 + (core + step_core) % 2))
    return pairs


def partial_integrals(left_block, right_block):
    return lax.dot_general(
        left_block, right_block, (((0,), (0,)), ((), ())), preferred_element_type=jnp.float32
    )


def contribution(right_block, amplitude):
    return lax.dot_general(
        right_block, amplitude, (((1,), (1,)), ((), ())), preferred_element_type=jnp.float32
    )


def per_device(b_rows, b_cols, eps_occ, eps_va, eps_vb):
    per_block = b_rows.shape[1] // eps_va.shape[0]
    cycle_size = lax.axis_size("occ")
    position = lax.axis_index("occ")
    aux_size = lax.axis_size("aux")
    aux_pos = lax.axis_index("aux")
    core = aux_pos % 2
    chips = aux_size // 2
    rows = b_rows.shape[1]
    half = rows // 2

    def energy(offset, virt_energy):
        which = (position + offset) % cycle_size
        occ_energy = lax.dynamic_slice_in_dim(eps_occ, which * per_block, per_block)
        return (virt_energy[None, :] - occ_energy[:, None]).reshape(-1)

    col_energy = energy(0, eps_vb)

    def amplitude(partial, shift):
        give = lax.dynamic_slice_in_dim(partial, (1 - core) * half, half, 0)
        keep = lax.dynamic_slice_in_dim(partial, core * half, half, 0)
        got = lax.ppermute(give, "aux", aux_pairs(aux_size, 1, 0))
        summed = keep + got
        others = [lax.ppermute(summed, "aux", aux_pairs(aux_size, 0, d)) for d in range(1, chips)]
        for other in others:
            summed = summed + other
        row_energy = lax.dynamic_slice_in_dim(energy(shift, eps_va), core * half, half, 0)
        amp_half = (spin_scale * summed / (row_energy[:, None] + col_energy[None, :])).astype(jnp.bfloat16)
        amp_other = lax.ppermute(amp_half, "aux", aux_pairs(aux_size, 1, 0))
        first = jnp.concatenate([amp_half, amp_other], axis=0)
        second = jnp.concatenate([amp_other, amp_half], axis=0)
        return jnp.where(core == 0, first, second)

    rows_1 = shifted(b_rows, "occ", -1)
    rows_2 = shifted(rows_1, "occ", -1)
    pieces = []
    for shift, left in enumerate([b_rows, rows_1, rows_2]):
        amp = amplitude(partial_integrals(left, b_cols), shift)
        pieces.append(contribution(b_cols, amp))
    carried = shifted(pieces[2], "occ", 1)
    carried = shifted(pieces[1] + carried, "occ", 1)
    return pieces[0] + carried


def solution(mesh):
    return jax.shard_map(
        per_device,
        mesh=mesh,
        in_specs=(P("aux", "occ"), P("aux", "occ"), P(), P(), P()),
        out_specs=P("aux", "occ"),
        check_vma=False,
    )
```

```python
import jax
import jax.numpy as jnp
from jax import lax
from jax.sharding import PartitionSpec as P

spin_scale = 1.3


def shifted(value, axis, by):
    size = lax.axis_size(axis)
    return lax.ppermute(value, axis, [(i, (i + by) % size) for i in range(size)])


def aux_pairs(size, step_core, step_chip):
    pairs = []
    for i in range(size):
        chip, core = divmod(i, 2)
        chips = size // 2
        pairs.append((i, ((chip + step_chip) % chips) * 2 + (core + step_core) % 2))
    return pairs


def partial_integrals(left_block, right_block):
    return lax.dot_general(
        left_block, right_block, (((0,), (0,)), ((), ())), preferred_element_type=jnp.float32
    )


def contribution(right_block, amplitude):
    return lax.dot_general(
        right_block, amplitude, (((1,), (1,)), ((), ())), preferred_element_type=jnp.float32
    )


def per_device(b_rows, b_cols, eps_occ, eps_va, eps_vb):
    per_block = b_rows.shape[1] // eps_va.shape[0]
    cycle_size = lax.axis_size("occ")
    position = lax.axis_index("occ")
    aux_size = lax.axis_size("aux")
    aux_pos = lax.axis_index("aux")
    core = aux_pos % 2
    chips = aux_size // 2
    rows = b_rows.shape[1]
    half = rows // 2

    def energy(offset, virt_energy):
        which = (position + offset) % cycle_size
        occ_energy = lax.dynamic_slice_in_dim(eps_occ, which * per_block, per_block)
        return (virt_energy[None, :] - occ_energy[:, None]).reshape(-1)

    col_energy = energy(0, eps_vb)

    def core_reduce(partials):
        stack = jnp.stack(partials)
        give = lax.dynamic_slice_in_dim(stack, (1 - core) * half, half, 1)
        keep = lax.dynamic_slice_in_dim(stack, core * half, half, 1)
        return keep + lax.ppermute(give, "aux", aux_pairs(aux_size, 1, 0))

    def chip_reduce(summed):
        others = [lax.ppermute(summed, "aux", aux_pairs(aux_size, 0, d)) for d in range(1, chips)]
        for other in others:
            summed = summed + other
        return summed

    def amplitude_half(summed, shift):
        row_energy = lax.dynamic_slice_in_dim(energy(shift, eps_va), core * half, half, 0)
        return (spin_scale * summed / (row_energy[:, None] + col_energy[None, :])).astype(jnp.bfloat16)

    rows_1 = shifted(b_rows, "occ", -1)
    early = chip_reduce(core_reduce([partial_integrals(b_rows, b_cols), partial_integrals(rows_1, b_cols)]))
    rows_2 = shifted(rows_1, "occ", -1)
    late = chip_reduce(core_reduce([partial_integrals(rows_2, b_cols)]))
    amp_halves = jnp.stack([amplitude_half(early[0], 0), amplitude_half(early[1], 1), amplitude_half(late[0], 2)])
    amp_other = lax.ppermute(amp_halves, "aux", aux_pairs(aux_size, 1, 0))
    first = jnp.concatenate([amp_halves, amp_other], axis=1)
    second = jnp.concatenate([amp_other, amp_halves], axis=1)
    amps = jnp.where(core == 0, first, second)
    pieces = [contribution(b_cols, amps[s]) for s in range(3)]
    carried = shifted(pieces[2], "occ", 1)
    carried = shifted(pieces[1] + carried, "occ", 1)
    return pieces[0] + carried


def solution(mesh):
    return jax.shard_map(
        per_device,
        mesh=mesh,
        in_specs=(P("aux", "occ"), P("aux", "occ"), P(), P(), P()),
        out_specs=P("aux", "occ"),
        check_vma=False,
    )
```

```python
import jax
import jax.numpy as jnp
from jax import lax
from jax.sharding import PartitionSpec as P

spin_scale = 1.3


def shifted(value, axis, by):
    size = lax.axis_size(axis)
    return lax.ppermute(value, axis, [(i, (i + by) % size) for i in range(size)])


def aux_pairs(size, step_core, step_chip):
    pairs = []
    for i in range(size):
        chip, core = divmod(i, 2)
        chips = size // 2
        pairs.append((i, ((chip + step_chip) % chips) * 2 + (core + step_core) % 2))
    return pairs


def partial_integrals(left_block, right_block):
    return lax.dot_general(
        left_block, right_block, (((0,), (0,)), ((), ())), preferred_element_type=jnp.float32
    )


def contribution(right_block, amplitude):
    return lax.dot_general(
        right_block, amplitude, (((1,), (1,)), ((), ())), preferred_element_type=jnp.float32
    )


def per_device(b_rows, b_cols, eps_occ, eps_va, eps_vb):
    per_block = b_rows.shape[1] // eps_va.shape[0]
    cycle_size = lax.axis_size("occ")
    position = lax.axis_index("occ")
    aux_size = lax.axis_size("aux")
    aux_pos = lax.axis_index("aux")
    core = aux_pos % 2
    chips = aux_size // 2
    rows = b_rows.shape[1]
    half = rows // 2

    def energy(offset, virt_energy):
        which = (position + offset) % cycle_size
        occ_energy = lax.dynamic_slice_in_dim(eps_occ, which * per_block, per_block)
        return (virt_energy[None, :] - occ_energy[:, None]).reshape(-1)

    def core_reduce(partials):
        stack = jnp.stack(partials)
        give = lax.dynamic_slice_in_dim(stack, (1 - core) * half, half, 1)
        keep = lax.dynamic_slice_in_dim(stack, core * half, half, 1)
        return keep + lax.ppermute(give, "aux", aux_pairs(aux_size, 1, 0))

    def chip_reduce(summed):
        others = [lax.ppermute(summed, "aux", aux_pairs(aux_size, 0, d)) for d in range(1, chips)]
        for other in others:
            summed = summed + other
        return summed

    def amplitude_half(summed, row_shift, col_shift):
        row_energy = lax.dynamic_slice_in_dim(energy(row_shift, eps_va), core * half, half, 0)
        col_energy = energy(col_shift, eps_vb)
        return (spin_scale * summed / (row_energy[:, None] + col_energy[None, :])).astype(jnp.bfloat16)

    cols_prev = shifted(b_cols, "occ", 1)
    rows_next = shifted(b_rows, "occ", -1)
    early = chip_reduce(core_reduce([partial_integrals(b_rows, b_cols), partial_integrals(rows_next, b_cols)]))
    late = chip_reduce(core_reduce([partial_integrals(rows_next, cols_prev)]))
    amp_halves = jnp.stack([
        amplitude_half(early[0], 0, 0), amplitude_half(early[1], 1, 0), amplitude_half(late[0], 1, -1)
    ])
    amp_other = lax.ppermute(amp_halves, "aux", aux_pairs(aux_size, 1, 0))
    first = jnp.concatenate([amp_halves, amp_other], axis=1)
    second = jnp.concatenate([amp_other, amp_halves], axis=1)
    amps = jnp.where(core == 0, first, second)
    own = contribution(b_cols, amps[0])
    onward = contribution(b_cols, amps[1]) + contribution(cols_prev, amps[2])
    return own + shifted(onward, "occ", 1)


def solution(mesh):
    return jax.shard_map(
        per_device,
        mesh=mesh,
        in_specs=(P("aux", "occ"), P("aux", "occ"), P(), P(), P()),
        out_specs=P("aux", "occ"),
        check_vma=False,
    )
```

```python
import jax
import jax.numpy as jnp
from jax import lax
from jax.sharding import PartitionSpec as P

spin_scale = 1.3


def shifted(value, axis, by):
    size = lax.axis_size(axis)
    return lax.ppermute(value, axis, [(i, (i + by) % size) for i in range(size)])


def aux_pairs(size, step_core, step_chip):
    pairs = []
    for i in range(size):
        chip, core = divmod(i, 2)
        chips = size // 2
        pairs.append((i, ((chip + step_chip) % chips) * 2 + (core + step_core) % 2))
    return pairs


def partial_integrals(left_block, right_block):
    return lax.dot_general(
        left_block, right_block, (((0,), (0,)), ((), ())), preferred_element_type=jnp.float32
    )


def contribution(right_block, amplitude):
    return lax.dot_general(
        right_block, amplitude, (((1,), (1,)), ((), ())), preferred_element_type=jnp.float32
    )


def per_device(b_rows, b_cols, eps_occ, eps_va, eps_vb):
    per_block = b_rows.shape[1] // eps_va.shape[0]
    cycle_size = lax.axis_size("occ")
    position = lax.axis_index("occ")
    aux_size = lax.axis_size("aux")
    aux_pos = lax.axis_index("aux")
    core = aux_pos % 2
    chips = aux_size // 2
    rows = b_rows.shape[1]
    half = rows // 2

    def energy(offset, virt_energy):
        which = (position + offset) % cycle_size
        occ_energy = lax.dynamic_slice_in_dim(eps_occ, which * per_block, per_block)
        return (virt_energy[None, :] - occ_energy[:, None]).reshape(-1)

    def core_reduce(partials):
        stack = jnp.stack(partials)
        give = lax.dynamic_slice_in_dim(stack, (1 - core) * half, half, 1)
        keep = lax.dynamic_slice_in_dim(stack, core * half, half, 1)
        return keep + lax.ppermute(give, "aux", aux_pairs(aux_size, 1, 0))

    chip = aux_pos // 2
    piece = -(-half // chips)
    piece = -(-piece // 8) * 8

    def chip_reduce(summed):
        padded = jnp.pad(summed, ((0, 0), (0, piece * chips - half), (0, 0)))
        parts = padded.reshape(padded.shape[0], chips, piece, padded.shape[2])
        mine = lax.dynamic_index_in_dim(parts, chip, 1, keepdims=False)
        for d in range(1, chips):
            give = lax.dynamic_index_in_dim(parts, (chip + d) % chips, 1, keepdims=False)
            mine = mine + lax.ppermute(give, "aux", aux_pairs(aux_size, 0, d))
        return mine

    def chip_gather(mine):
        whole = jnp.zeros((mine.shape[0], chips, piece, mine.shape[2]), mine.dtype)
        whole = lax.dynamic_update_index_in_dim(whole, mine, chip, 1)
        for d in range(1, chips):
            got = lax.ppermute(mine, "aux", aux_pairs(aux_size, 0, d))
            whole = lax.dynamic_update_index_in_dim(whole, got, (chip - d) % chips, 1)
        return whole.reshape(mine.shape[0], chips * piece, mine.shape[2])[:, :half]

    def amplitude_part(summed, row_shift):
        row_energy = lax.dynamic_slice_in_dim(energy(row_shift, eps_va), core * half, half, 0)
        row_energy = jnp.pad(row_energy, (0, piece * chips - half), constant_values=1.0)
        row_energy = lax.dynamic_slice_in_dim(row_energy, chip * piece, piece, 0)
        col_energy = energy(0, eps_vb)
        return (spin_scale * summed / (row_energy[:, None] + col_energy[None, :])).astype(jnp.bfloat16)

    def core_gather(halves):
        other = lax.ppermute(halves, "aux", aux_pairs(aux_size, 1, 0))
        first = jnp.concatenate([halves, other], axis=1)
        second = jnp.concatenate([other, halves], axis=1)
        return jnp.where(core == 0, first, second)

    cols_prev = shifted(b_cols, "occ", 1)
    rows_next = shifted(b_rows, "occ", -1)
    rows_after = shifted(rows_next, "occ", -1)
    lefts = [b_rows, rows_next, rows_after]
    summed = chip_reduce(core_reduce([partial_integrals(left, b_cols) for left in lefts]))
    amp_halves = chip_gather(jnp.stack([amplitude_part(summed[s], s) for s in range(3)]))
    far = shifted(amp_halves[2], "occ", 1)
    amps = core_gather(jnp.stack([amp_halves[0], amp_halves[1], far]))
    own = contribution(b_cols, amps[0])
    onward = contribution(b_cols, amps[1]) + contribution(cols_prev, amps[2])
    return own + shifted(onward, "occ", 1)


def solution(mesh):
    return jax.shard_map(
        per_device,
        mesh=mesh,
        in_specs=(P("aux", "occ"), P("aux", "occ"), P(), P(), P()),
        out_specs=P("aux", "occ"),
        check_vma=False,
    )
```

```python
import jax
import jax.numpy as jnp
from jax import lax
from jax.sharding import PartitionSpec as P

spin_scale = 1.3


def shifted(value, axis, by):
    size = lax.axis_size(axis)
    return lax.ppermute(value, axis, [(i, (i + by) % size) for i in range(size)])


def aux_pairs(size, step_core, step_chip):
    pairs = []
    for i in range(size):
        chip, core = divmod(i, 2)
        chips = size // 2
        pairs.append((i, ((chip + step_chip) % chips) * 2 + (core + step_core) % 2))
    return pairs


def partial_integrals(left_block, right_block):
    return lax.dot_general(
        left_block, right_block, (((0,), (0,)), ((), ())), preferred_element_type=jnp.float32
    )


def contribution(right_block, amplitude):
    return lax.dot_general(
        right_block, amplitude, (((1,), (1,)), ((), ())), preferred_element_type=jnp.float32
    )


def per_device(b_rows, b_cols, eps_occ, eps_va, eps_vb):
    per_block = b_rows.shape[1] // eps_va.shape[0]
    cycle_size = lax.axis_size("occ")
    position = lax.axis_index("occ")
    aux_size = lax.axis_size("aux")
    aux_pos = lax.axis_index("aux")
    core = aux_pos % 2
    chips = aux_size // 2
    rows = b_rows.shape[1]
    half = rows // 2

    def energy(offset, virt_energy):
        which = (position + offset) % cycle_size
        occ_energy = lax.dynamic_slice_in_dim(eps_occ, which * per_block, per_block)
        return (virt_energy[None, :] - occ_energy[:, None]).reshape(-1)

    def core_reduce(partials):
        stack = jnp.stack(partials)
        give = lax.dynamic_slice_in_dim(stack, (1 - core) * half, half, 1)
        keep = lax.dynamic_slice_in_dim(stack, core * half, half, 1)
        return keep + lax.ppermute(give, "aux", aux_pairs(aux_size, 1, 0))

    chip = aux_pos // 2
    piece = -(-half // chips)
    piece = -(-piece // 8) * 8

    def chip_reduce(summed):
        padded = jnp.pad(summed, ((0, 0), (0, piece * chips - half), (0, 0)))
        parts = padded.reshape(padded.shape[0], chips, piece, padded.shape[2])
        mine = lax.dynamic_index_in_dim(parts, chip, 1, keepdims=False)
        for d in range(1, chips):
            give = lax.dynamic_index_in_dim(parts, (chip + d) % chips, 1, keepdims=False)
            mine = mine + lax.ppermute(give, "aux", aux_pairs(aux_size, 0, d))
        return mine

    def chip_gather(mine):
        whole = jnp.zeros((mine.shape[0], chips, piece, mine.shape[2]), mine.dtype)
        whole = lax.dynamic_update_index_in_dim(whole, mine, chip, 1)
        for d in range(1, chips):
            got = lax.ppermute(mine, "aux", aux_pairs(aux_size, 0, d))
            whole = lax.dynamic_update_index_in_dim(whole, got, (chip - d) % chips, 1)
        return whole.reshape(mine.shape[0], chips * piece, mine.shape[2])[:, :half]

    def amplitude_part(summed, row_shift):
        row_energy = lax.dynamic_slice_in_dim(energy(row_shift, eps_va), core * half, half, 0)
        row_energy = jnp.pad(row_energy, (0, piece * chips - half), constant_values=1.0)
        row_energy = lax.dynamic_slice_in_dim(row_energy, chip * piece, piece, 0)
        col_energy = energy(0, eps_vb)
        return (spin_scale * summed / (row_energy[:, None] + col_energy[None, :])).astype(jnp.bfloat16)

    def core_gather(halves):
        other = lax.ppermute(halves, "aux", aux_pairs(aux_size, 1, 0))
        first = jnp.concatenate([halves, other], axis=1)
        second = jnp.concatenate([other, halves], axis=1)
        return jnp.where(core == 0, first, second)

    def chip_exchange(summed):
        others = [lax.ppermute(summed, "aux", aux_pairs(aux_size, 0, d)) for d in range(1, chips)]
        for other in others:
            summed = summed + other
        return summed

    def amplitude_half(summed, row_shift, col_shift):
        row_energy = lax.dynamic_slice_in_dim(energy(row_shift, eps_va), core * half, half, 0)
        col_energy = energy(col_shift, eps_vb)
        return (spin_scale * summed / (row_energy[:, None] + col_energy[None, :])).astype(jnp.bfloat16)

    cols_prev = shifted(b_cols, "occ", 1)
    rows_next = shifted(b_rows, "occ", -1)
    early = chip_reduce(core_reduce([partial_integrals(b_rows, b_cols), partial_integrals(rows_next, b_cols)]))
    early_amps = chip_gather(jnp.stack([amplitude_part(early[0], 0), amplitude_part(early[1], 1)]))
    late = chip_exchange(core_reduce([partial_integrals(rows_next, cols_prev)]))
    amp_halves = jnp.concatenate([early_amps, amplitude_half(late[0], 1, -1)[None]])
    amps = core_gather(amp_halves)
    own = contribution(b_cols, amps[0])
    onward = contribution(b_cols, amps[1]) + contribution(cols_prev, amps[2])
    return own + shifted(onward, "occ", 1)


def solution(mesh):
    return jax.shard_map(
        per_device,
        mesh=mesh,
        in_specs=(P("aux", "occ"), P("aux", "occ"), P(), P(), P()),
        out_specs=P("aux", "occ"),
        check_vma=False,
    )
```

```python
import jax
import jax.numpy as jnp
from jax import lax
from jax.sharding import PartitionSpec as P

spin_scale = 1.3


def shifted(value, axis, by):
    size = lax.axis_size(axis)
    return lax.ppermute(value, axis, [(i, (i + by) % size) for i in range(size)])


def partial_integrals(left_block, right_block):
    return lax.dot_general(
        left_block, right_block, (((0,), (0,)), ((), ())), preferred_element_type=jnp.float32
    )


def contribution(right_block, amplitude):
    return lax.dot_general(
        right_block, amplitude, (((1,), (1,)), ((), ())), preferred_element_type=jnp.float32
    )


def per_device(b_rows, b_cols, eps_occ, eps_va, eps_vb):
    per_block = b_rows.shape[1] // eps_va.shape[0]
    cycle_size = lax.axis_size("occ")
    position = lax.axis_index("occ")
    aux_size = lax.axis_size("aux")
    aux_pos = lax.axis_index("aux")
    rows = b_rows.shape[1]

    def energy(offset, virt_energy):
        which = (position + offset) % cycle_size
        occ_energy = lax.dynamic_slice_in_dim(eps_occ, which * per_block, per_block)
        return (virt_energy[None, :] - occ_energy[:, None]).reshape(-1)

    piece = -(-rows // aux_size)
    piece = -(-piece // 8) * 8
    padded_rows = piece * aux_size

    def aux_reduce(partials):
        stack = jnp.pad(jnp.stack(partials), ((0, 0), (0, padded_rows - rows), (0, 0)))
        parts = stack.reshape(stack.shape[0], aux_size, piece, stack.shape[2])
        got = lax.all_to_all(parts, "aux", 1, 1, tiled=True)
        return got.sum(axis=1)

    def aux_gather(mine):
        spread = jnp.broadcast_to(mine[:, None], (mine.shape[0], aux_size) + mine.shape[1:])
        got = lax.all_to_all(spread, "aux", 1, 1, tiled=True)
        return got.reshape(mine.shape[0], padded_rows, mine.shape[2])[:, :rows]

    def amplitude_part(summed, row_shift):
        row_energy = jnp.pad(energy(row_shift, eps_va), (0, padded_rows - rows), constant_values=1.0)
        row_energy = lax.dynamic_slice_in_dim(row_energy, aux_pos * piece, piece, 0)
        col_energy = energy(0, eps_vb)
        return (spin_scale * summed / (row_energy[:, None] + col_energy[None, :])).astype(jnp.bfloat16)

    cols_prev = shifted(b_cols, "occ", 1)
    rows_next = shifted(b_rows, "occ", -1)
    rows_after = shifted(rows_next, "occ", -1)
    lefts = [b_rows, rows_next, rows_after]
    summed = aux_reduce([partial_integrals(left, b_cols) for left in lefts])
    amp_parts = [amplitude_part(summed[s], s) for s in range(3)]
    far = shifted(amp_parts[2], "occ", 1)
    amps = aux_gather(jnp.stack([amp_parts[0], amp_parts[1], far]))
    own = contribution(b_cols, amps[0])
    onward = contribution(b_cols, amps[1]) + contribution(cols_prev, amps[2])
    return own + shifted(onward, "occ", 1)


def solution(mesh):
    return jax.shard_map(
        per_device,
        mesh=mesh,
        in_specs=(P("aux", "occ"), P("aux", "occ"), P(), P(), P()),
        out_specs=P("aux", "occ"),
        check_vma=False,
    )
```

```python
import jax
import jax.numpy as jnp
from jax import lax
from jax.sharding import PartitionSpec as P

spin_scale = 1.3


def shifted(value, axis, by):
    size = lax.axis_size(axis)
    return lax.ppermute(value, axis, [(i, (i + by) % size) for i in range(size)])


def aux_pairs(size, step_core, step_chip):
    pairs = []
    for i in range(size):
        chip, core = divmod(i, 2)
        chips = size // 2
        pairs.append((i, ((chip + step_chip) % chips) * 2 + (core + step_core) % 2))
    return pairs


def partial_integrals(left_block, right_block):
    return lax.dot_general(
        left_block, right_block, (((0,), (0,)), ((), ())), preferred_element_type=jnp.float32
    )


def contribution(right_block, amplitude):
    return lax.dot_general(
        right_block, amplitude, (((1,), (1,)), ((), ())), preferred_element_type=jnp.float32
    )


def per_device(b_rows, b_cols, eps_occ, eps_va, eps_vb):
    per_block = b_rows.shape[1] // eps_va.shape[0]
    cycle_size = lax.axis_size("occ")
    position = lax.axis_index("occ")
    aux_size = lax.axis_size("aux")
    aux_pos = lax.axis_index("aux")
    core = aux_pos % 2
    chips = aux_size // 2
    rows = b_rows.shape[1]
    half = rows // 2

    def energy(offset, virt_energy):
        which = (position + offset) % cycle_size
        occ_energy = lax.dynamic_slice_in_dim(eps_occ, which * per_block, per_block)
        return (virt_energy[None, :] - occ_energy[:, None]).reshape(-1)

    def core_reduce(partials):
        stack = jnp.stack(partials)
        give = lax.dynamic_slice_in_dim(stack, (1 - core) * half, half, 1)
        keep = lax.dynamic_slice_in_dim(stack, core * half, half, 1)
        return keep + lax.ppermute(give, "aux", aux_pairs(aux_size, 1, 0))

    def chip_reduce(summed):
        others = [lax.ppermute(summed, "aux", aux_pairs(aux_size, 0, d)) for d in range(1, chips)]
        for other in others:
            summed = summed + other
        return summed

    def amplitude_half(summed, row_shift, col_shift):
        row_energy = lax.dynamic_slice_in_dim(energy(row_shift, eps_va), core * half, half, 0)
        col_energy = energy(col_shift, eps_vb)
        return (spin_scale * summed / (row_energy[:, None] + col_energy[None, :])).astype(jnp.bfloat16)

    cols_prev = shifted(b_cols, "occ", 1)
    rows_next = shifted(b_rows, "occ", -1)
    early = chip_reduce(core_reduce([partial_integrals(b_rows, b_cols), partial_integrals(rows_next, b_cols)]))
    late = chip_reduce(core_reduce([partial_integrals(rows_next, cols_prev)]))
    amp_halves = jnp.stack([
        amplitude_half(early[0], 0, 0), amplitude_half(early[1], 1, 0), amplitude_half(late[0], 1, -1)
    ])
    near_first = contribution(b_cols, amp_halves[1]) + contribution(cols_prev, amp_halves[2])
    sent_first = shifted(near_first, "occ", 1)
    amp_other = lax.ppermute(amp_halves, "aux", aux_pairs(aux_size, 1, 0))
    near_second = contribution(b_cols, amp_other[1]) + contribution(cols_prev, amp_other[2])
    sent_second = shifted(near_second, "occ", 1)
    first = jnp.concatenate([amp_halves[0], amp_other[0]], axis=0)
    second = jnp.concatenate([amp_other[0], amp_halves[0]], axis=0)
    own = contribution(b_cols, jnp.where(core == 0, first, second))
    sent = jnp.where(
        core == 0,
        jnp.concatenate([sent_first, sent_second], axis=1),
        jnp.concatenate([sent_second, sent_first], axis=1),
    )
    return own + sent


def solution(mesh):
    return jax.shard_map(
        per_device,
        mesh=mesh,
        in_specs=(P("aux", "occ"), P("aux", "occ"), P(), P(), P()),
        out_specs=P("aux", "occ"),
        check_vma=False,
    )
```

```python
import jax
import jax.numpy as jnp
from jax import lax
from jax.sharding import PartitionSpec as P

spin_scale = 1.3


def shifted(value, axis, by):
    size = lax.axis_size(axis)
    return lax.ppermute(value, axis, [(i, (i + by) % size) for i in range(size)])


def aux_pairs(size, step_core, step_chip):
    pairs = []
    for i in range(size):
        chip, core = divmod(i, 2)
        chips = size // 2
        pairs.append((i, ((chip + step_chip) % chips) * 2 + (core + step_core) % 2))
    return pairs


def partial_integrals(left_block, right_block):
    return lax.dot_general(
        left_block, right_block, (((0,), (0,)), ((), ())), preferred_element_type=jnp.float32
    )


def contribution(right_block, amplitude):
    return lax.dot_general(
        right_block, amplitude, (((1,), (1,)), ((), ())), preferred_element_type=jnp.float32
    )


def per_device(b_rows, b_cols, eps_occ, eps_va, eps_vb):
    per_block = b_rows.shape[1] // eps_va.shape[0]
    cycle_size = lax.axis_size("occ")
    position = lax.axis_index("occ")
    aux_size = lax.axis_size("aux")
    aux_pos = lax.axis_index("aux")
    core = aux_pos % 2
    chips = aux_size // 2
    rows = b_rows.shape[1]
    half = rows // 2

    def energy(offset, virt_energy):
        which = (position + offset) % cycle_size
        occ_energy = lax.dynamic_slice_in_dim(eps_occ, which * per_block, per_block)
        return (virt_energy[None, :] - occ_energy[:, None]).reshape(-1)

    def core_reduce(partials):
        stack = jnp.stack(partials)
        give = lax.dynamic_slice_in_dim(stack, (1 - core) * half, half, 1)
        keep = lax.dynamic_slice_in_dim(stack, core * half, half, 1)
        return keep + lax.ppermute(give, "aux", aux_pairs(aux_size, 1, 0))

    def chip_reduce(summed):
        others = [lax.ppermute(summed, "aux", aux_pairs(aux_size, 0, d)) for d in range(1, chips)]
        for other in others:
            summed = summed + other
        return summed

    def amplitude_half(summed, row_shift, col_shift):
        row_energy = lax.dynamic_slice_in_dim(energy(row_shift, eps_va), core * half, half, 0)
        col_energy = energy(col_shift, eps_vb)
        return (spin_scale * summed / (row_energy[:, None] + col_energy[None, :])).astype(jnp.bfloat16)

    cols_prev = shifted(b_cols, "occ", 1)
    rows_next = shifted(b_rows, "occ", -1)
    with jax.named_scope("own_sum"):
        early = chip_reduce(core_reduce([partial_integrals(b_rows, b_cols)]))
    late = chip_reduce(core_reduce([partial_integrals(rows_next, cols_prev)]))
    far_half = amplitude_half(late[0], 1, -1)
    with jax.named_scope("hop_a"):
        sent_first = shifted(contribution(cols_prev, far_half), "occ", 1)
    far_other = lax.ppermute(far_half, "aux", aux_pairs(aux_size, 1, 0))
    far_second = contribution(cols_prev, far_other)
    with jax.named_scope("hop_b"):
        sent_second = shifted(far_second, "occ", 1)
    near_partial = partial_integrals(b_rows, cols_prev)
    with jax.named_scope("near_sum"):
        near = chip_reduce(core_reduce([near_partial]))
    amp_halves = jnp.stack([amplitude_half(early[0], 0, 0), amplitude_half(near[0], 0, -1)])
    amp_other = lax.ppermute(amp_halves, "aux", aux_pairs(aux_size, 1, 0))
    first = jnp.concatenate([amp_halves, amp_other], axis=1)
    second = jnp.concatenate([amp_other, amp_halves], axis=1)
    amps = jnp.where(core == 0, first, second)
    own = contribution(b_cols, amps[0]) + contribution(cols_prev, amps[1])
    sent = jnp.where(
        core == 0,
        jnp.concatenate([sent_first, sent_second], axis=1),
        jnp.concatenate([sent_second, sent_first], axis=1),
    )
    return own + sent


def solution(mesh):
    return jax.shard_map(
        per_device,
        mesh=mesh,
        in_specs=(P("aux", "occ"), P("aux", "occ"), P(), P(), P()),
        out_specs=P("aux", "occ"),
        check_vma=False,
    )
```

```python
import jax
import jax.numpy as jnp
from jax import lax
from jax.sharding import PartitionSpec as P

spin_scale = 1.3


def shifted(value, axis, by):
    size = lax.axis_size(axis)
    return lax.ppermute(value, axis, [(i, (i + by) % size) for i in range(size)])


def aux_pairs(size, step_core, step_chip):
    pairs = []
    for i in range(size):
        chip, core = divmod(i, 2)
        chips = size // 2
        pairs.append((i, ((chip + step_chip) % chips) * 2 + (core + step_core) % 2))
    return pairs


def partial_integrals(left_block, right_block):
    return lax.dot_general(
        left_block, right_block, (((0,), (0,)), ((), ())), preferred_element_type=jnp.float32
    )


def contribution(right_block, amplitude):
    return lax.dot_general(
        right_block, amplitude, (((1,), (1,)), ((), ())), preferred_element_type=jnp.float32
    )


def per_device(b_rows, b_cols, eps_occ, eps_va, eps_vb):
    per_block = b_rows.shape[1] // eps_va.shape[0]
    cycle_size = lax.axis_size("occ")
    position = lax.axis_index("occ")
    aux_size = lax.axis_size("aux")
    aux_pos = lax.axis_index("aux")
    core = aux_pos % 2
    chips = aux_size // 2
    rows = b_rows.shape[1]
    half = rows // 2

    def energy(offset, virt_energy):
        which = (position + offset) % cycle_size
        occ_energy = lax.dynamic_slice_in_dim(eps_occ, which * per_block, per_block)
        return (virt_energy[None, :] - occ_energy[:, None]).reshape(-1)

    def core_reduce(partials):
        stack = jnp.stack(partials)
        give = lax.dynamic_slice_in_dim(stack, (1 - core) * half, half, 1)
        keep = lax.dynamic_slice_in_dim(stack, core * half, half, 1)
        return keep + lax.ppermute(give, "aux", aux_pairs(aux_size, 1, 0))

    def chip_reduce(summed):
        others = [lax.ppermute(summed, "aux", aux_pairs(aux_size, 0, d)) for d in range(1, chips)]
        for other in others:
            summed = summed + other
        return summed

    def amplitude_half(summed, row_shift, col_shift):
        row_energy = lax.dynamic_slice_in_dim(energy(row_shift, eps_va), core * half, half, 0)
        col_energy = energy(col_shift, eps_vb)
        return (spin_scale * summed / (row_energy[:, None] + col_energy[None, :])).astype(jnp.bfloat16)

    def core_gather(halves):
        other = lax.ppermute(halves, "aux", aux_pairs(aux_size, 1, 0))
        first = jnp.concatenate([halves, other], axis=1)
        second = jnp.concatenate([other, halves], axis=1)
        return jnp.where(core == 0, first, second)

    cols_prev = shifted(b_cols, "occ", 1)
    rows_next = shifted(b_rows, "occ", -1)
    rows_after = shifted(rows_next, "occ", -1)
    own_sum = chip_reduce(core_reduce([partial_integrals(b_rows, b_cols)]))
    own_amp = core_gather(amplitude_half(own_sum[0], 0, 0)[None])
    ahead = chip_reduce(core_reduce([partial_integrals(rows_next, b_cols), partial_integrals(rows_after, b_cols)]))
    amp_near = amplitude_half(ahead[0], 1, 0)
    amp_far = shifted(amplitude_half(ahead[1], 2, 0), "occ", 1)
    amps = core_gather(jnp.stack([amp_near, amp_far]))
    onward = contribution(b_cols, amps[0]) + contribution(cols_prev, amps[1])
    sent = shifted(onward, "occ", 1)
    return contribution(b_cols, own_amp[0]) + sent


def solution(mesh):
    return jax.shard_map(
        per_device,
        mesh=mesh,
        in_specs=(P("aux", "occ"), P("aux", "occ"), P(), P(), P()),
        out_specs=P("aux", "occ"),
        check_vma=False,
    )
```

```python
import jax
import jax.numpy as jnp
from jax import lax
from jax.sharding import PartitionSpec as P

spin_scale = 1.3


def shifted(value, axis, by):
    size = lax.axis_size(axis)
    return lax.ppermute(value, axis, [(i, (i + by) % size) for i in range(size)])


def aux_pairs(size, step_core, step_chip):
    pairs = []
    for i in range(size):
        chip, core = divmod(i, 2)
        chips = size // 2
        pairs.append((i, ((chip + step_chip) % chips) * 2 + (core + step_core) % 2))
    return pairs


def partial_integrals(left_block, right_block):
    return lax.dot_general(
        left_block, right_block, (((0,), (0,)), ((), ())), preferred_element_type=jnp.float32
    )


def contribution(right_block, amplitude):
    return lax.dot_general(
        right_block, amplitude, (((1,), (1,)), ((), ())), preferred_element_type=jnp.float32
    )


def per_device(b_rows, b_cols, eps_occ, eps_va, eps_vb):
    per_block = b_rows.shape[1] // eps_va.shape[0]
    cycle_size = lax.axis_size("occ")
    position = lax.axis_index("occ")
    aux_size = lax.axis_size("aux")
    aux_pos = lax.axis_index("aux")
    core = aux_pos % 2
    chips = aux_size // 2
    rows = b_rows.shape[1]
    half = rows // 2

    def energy(offset, virt_energy):
        which = (position + offset) % cycle_size
        occ_energy = lax.dynamic_slice_in_dim(eps_occ, which * per_block, per_block)
        return (virt_energy[None, :] - occ_energy[:, None]).reshape(-1)

    def core_reduce(partials):
        stack = jnp.stack(partials)
        give = lax.dynamic_slice_in_dim(stack, (1 - core) * half, half, 1)
        keep = lax.dynamic_slice_in_dim(stack, core * half, half, 1)
        return keep + lax.ppermute(give, "aux", aux_pairs(aux_size, 1, 0))

    def chip_reduce(summed):
        others = [lax.ppermute(summed, "aux", aux_pairs(aux_size, 0, d)) for d in range(1, chips)]
        for other in others:
            summed = summed + other
        return summed

    def amplitude_half(summed, row_shift, col_shift):
        row_energy = lax.dynamic_slice_in_dim(energy(row_shift, eps_va), core * half, half, 0)
        col_energy = energy(col_shift, eps_vb)
        return (spin_scale * summed / (row_energy[:, None] + col_energy[None, :])).astype(jnp.bfloat16)

    cols_prev = shifted(b_cols, "occ", 1)
    rows_next = shifted(b_rows, "occ", -1)
    early = chip_reduce(core_reduce([partial_integrals(b_rows, b_cols), partial_integrals(rows_next, b_cols)]))
    late = chip_reduce(core_reduce([partial_integrals(rows_next, cols_prev)]))
    early_halves = jnp.stack([amplitude_half(early[0], 0, 0), amplitude_half(early[1], 1, 0)])
    early_other = lax.ppermute(early_halves, "aux", aux_pairs(aux_size, 1, 0))
    first = jnp.concatenate([early_halves, early_other], axis=1)
    second = jnp.concatenate([early_other, early_halves], axis=1)
    early_amps = jnp.where(core == 0, first, second)
    own = contribution(b_cols, early_amps[0])
    near = contribution(b_cols, early_amps[1])
    lo = lax.dynamic_slice_in_dim(near, core * half, half, 1)
    hi = lax.dynamic_slice_in_dim(near, (1 - core) * half, half, 1)
    far_half = amplitude_half(late[0], 1, -1)
    sent_first = shifted(lo + contribution(cols_prev, far_half), "occ", 1)
    far_other = lax.ppermute(far_half, "aux", aux_pairs(aux_size, 1, 0))
    sent_second = shifted(hi + contribution(cols_prev, far_other), "occ", 1)
    sent = jnp.where(
        core == 0,
        jnp.concatenate([sent_first, sent_second], axis=1),
        jnp.concatenate([sent_second, sent_first], axis=1),
    )
    return own + sent


def solution(mesh):
    return jax.shard_map(
        per_device,
        mesh=mesh,
        in_specs=(P("aux", "occ"), P("aux", "occ"), P(), P(), P()),
        out_specs=P("aux", "occ"),
        check_vma=False,
    )
```

```python
import jax
import jax.numpy as jnp
from jax import lax
from jax.sharding import PartitionSpec as P

spin_scale = 1.3


def shifted(value, axis, by):
    size = lax.axis_size(axis)
    return lax.ppermute(value, axis, [(i, (i + by) % size) for i in range(size)])


def aux_pairs(size, step_core, step_chip):
    pairs = []
    for i in range(size):
        chip, core = divmod(i, 2)
        chips = size // 2
        pairs.append((i, ((chip + step_chip) % chips) * 2 + (core + step_core) % 2))
    return pairs


def partial_integrals(left_block, right_block):
    return lax.dot_general(
        left_block, right_block, (((0,), (0,)), ((), ())), preferred_element_type=jnp.float32
    )


def contribution(right_block, amplitude):
    return lax.dot_general(
        right_block, amplitude, (((1,), (1,)), ((), ())), preferred_element_type=jnp.float32
    )


def per_device(b_rows, b_cols, eps_occ, eps_va, eps_vb):
    per_block = b_rows.shape[1] // eps_va.shape[0]
    cycle_size = lax.axis_size("occ")
    position = lax.axis_index("occ")
    aux_size = lax.axis_size("aux")
    aux_pos = lax.axis_index("aux")
    core = aux_pos % 2
    chips = aux_size // 2
    rows = b_rows.shape[1]
    half = rows // 2

    def energy(offset, virt_energy):
        which = (position + offset) % cycle_size
        occ_energy = lax.dynamic_slice_in_dim(eps_occ, which * per_block, per_block)
        return (virt_energy[None, :] - occ_energy[:, None]).reshape(-1)

    def core_reduce(partials):
        stack = jnp.stack(partials)
        give = lax.dynamic_slice_in_dim(stack, (1 - core) * half, half, 1)
        keep = lax.dynamic_slice_in_dim(stack, core * half, half, 1)
        return keep + lax.ppermute(give, "aux", aux_pairs(aux_size, 1, 0))

    def chip_reduce(summed):
        others = [lax.ppermute(summed, "aux", aux_pairs(aux_size, 0, d)) for d in range(1, chips)]
        for other in others:
            summed = summed + other
        return summed

    def amplitude_half(summed, row_shift, col_shift):
        row_energy = lax.dynamic_slice_in_dim(energy(row_shift, eps_va), core * half, half, 0)
        col_energy = energy(col_shift, eps_vb)
        return (spin_scale * summed / (row_energy[:, None] + col_energy[None, :])).astype(jnp.bfloat16)

    cols_prev = shifted(b_cols, "occ", 1)
    rows_next = shifted(b_rows, "occ", -1)
    early_core = core_reduce([partial_integrals(b_rows, b_cols), partial_integrals(rows_next, b_cols)])
    late_core = core_reduce([partial_integrals(rows_next, cols_prev)])
    early_core, late_core = lax.optimization_barrier((early_core, late_core))
    summed = chip_reduce(jnp.concatenate([early_core, late_core]))
    early, late = summed[:2], summed[2:]
    amp_halves = jnp.stack([
        amplitude_half(early[0], 0, 0), amplitude_half(early[1], 1, 0), amplitude_half(late[0], 1, -1)
    ])
    near_first = contribution(b_cols, amp_halves[1]) + contribution(cols_prev, amp_halves[2])
    sent_first = shifted(near_first, "occ", 1)
    amp_other = lax.ppermute(amp_halves, "aux", aux_pairs(aux_size, 1, 0))
    near_second = contribution(b_cols, amp_other[1]) + contribution(cols_prev, amp_other[2])
    sent_second = shifted(near_second, "occ", 1)
    first = jnp.concatenate([amp_halves[0], amp_other[0]], axis=0)
    second = jnp.concatenate([amp_other[0], amp_halves[0]], axis=0)
    own = contribution(b_cols, jnp.where(core == 0, first, second))
    sent = jnp.where(
        core == 0,
        jnp.concatenate([sent_first, sent_second], axis=1),
        jnp.concatenate([sent_second, sent_first], axis=1),
    )
    return own + sent


def solution(mesh):
    return jax.shard_map(
        per_device,
        mesh=mesh,
        in_specs=(P("aux", "occ"), P("aux", "occ"), P(), P(), P()),
        out_specs=P("aux", "occ"),
        check_vma=False,
    )
```

```python
import jax
import jax.numpy as jnp
from jax import lax
from jax.sharding import PartitionSpec as P

spin_scale = 1.3


def shifted(value, axis, by):
    size = lax.axis_size(axis)
    return lax.ppermute(value, axis, [(i, (i + by) % size) for i in range(size)])


def aux_pairs(size, step_core, step_chip):
    pairs = []
    for i in range(size):
        chip, core = divmod(i, 2)
        chips = size // 2
        pairs.append((i, ((chip + step_chip) % chips) * 2 + (core + step_core) % 2))
    return pairs


def partial_integrals(left_block, right_block):
    return lax.dot_general(
        left_block, right_block, (((0,), (0,)), ((), ())), preferred_element_type=jnp.float32
    )


def contribution(right_block, amplitude):
    return lax.dot_general(
        right_block, amplitude, (((1,), (1,)), ((), ())), preferred_element_type=jnp.float32
    )


def per_device(b_rows, b_cols, eps_occ, eps_va, eps_vb):
    per_block = b_rows.shape[1] // eps_va.shape[0]
    cycle_size = lax.axis_size("occ")
    position = lax.axis_index("occ")
    aux_size = lax.axis_size("aux")
    aux_pos = lax.axis_index("aux")
    core = aux_pos % 2
    chips = aux_size // 2
    rows = b_rows.shape[1]
    half = rows // 2

    def energy(offset, virt_energy):
        which = (position + offset) % cycle_size
        occ_energy = lax.dynamic_slice_in_dim(eps_occ, which * per_block, per_block)
        return (virt_energy[None, :] - occ_energy[:, None]).reshape(-1)

    def core_reduce(partials):
        stack = jnp.stack(partials)
        give = lax.dynamic_slice_in_dim(stack, (1 - core) * half, half, 1)
        keep = lax.dynamic_slice_in_dim(stack, core * half, half, 1)
        return keep + lax.ppermute(give, "aux", aux_pairs(aux_size, 1, 0))

    def chip_reduce(summed):
        others = [lax.ppermute(summed, "aux", aux_pairs(aux_size, 0, d)) for d in range(1, chips)]
        for other in others:
            summed = summed + other
        return summed

    def amplitude_half(summed, row_shift, col_shift):
        row_energy = lax.dynamic_slice_in_dim(energy(row_shift, eps_va), core * half, half, 0)
        col_energy = energy(col_shift, eps_vb)
        return (spin_scale * summed / (row_energy[:, None] + col_energy[None, :])).astype(jnp.bfloat16)

    cols_prev = shifted(b_cols, "occ", 1)
    rows_next = shifted(b_rows, "occ", -1)
    early_core = core_reduce([partial_integrals(b_rows, b_cols), partial_integrals(rows_next, b_cols)])
    late_core = core_reduce([partial_integrals(rows_next, cols_prev)])
    early_core, late_core = lax.optimization_barrier((early_core, late_core))
    chip = aux_pos // 2
    piece = -(-(-(-half // chips)) // 8) * 8
    padded = jnp.pad(jnp.concatenate([early_core, late_core]), ((0, 0), (0, piece * chips - half), (0, 0)))
    parts = padded.reshape(padded.shape[0], chips, piece, padded.shape[2])
    mine = lax.dynamic_index_in_dim(parts, chip, 1, keepdims=False)
    for d in range(1, chips):
        give = lax.dynamic_index_in_dim(parts, (chip + d) % chips, 1, keepdims=False)
        mine = mine + lax.ppermute(give, "aux", aux_pairs(aux_size, 0, d))

    def amplitude_part(summed, row_shift, col_shift):
        row_energy = lax.dynamic_slice_in_dim(energy(row_shift, eps_va), core * half, half, 0)
        row_energy = jnp.pad(row_energy, (0, piece * chips - half), constant_values=1.0)
        row_energy = lax.dynamic_slice_in_dim(row_energy, chip * piece, piece, 0)
        col_energy = energy(col_shift, eps_vb)
        return (spin_scale * summed / (row_energy[:, None] + col_energy[None, :])).astype(jnp.bfloat16)

    amp_mine = jnp.stack([amplitude_part(mine[0], 0, 0), amplitude_part(mine[1], 1, 0), amplitude_part(mine[2], 1, -1)])
    whole = jnp.zeros((3, chips, piece, amp_mine.shape[2]), amp_mine.dtype)
    whole = lax.dynamic_update_index_in_dim(whole, amp_mine, chip, 1)
    for d in range(1, chips):
        got = lax.ppermute(amp_mine, "aux", aux_pairs(aux_size, 0, d))
        whole = lax.dynamic_update_index_in_dim(whole, got, (chip - d) % chips, 1)
    amp_halves = whole.reshape(3, chips * piece, amp_mine.shape[2])[:, :half]
    near_first = contribution(b_cols, amp_halves[1]) + contribution(cols_prev, amp_halves[2])
    sent_first = shifted(near_first, "occ", 1)
    amp_other = lax.ppermute(amp_halves, "aux", aux_pairs(aux_size, 1, 0))
    near_second = contribution(b_cols, amp_other[1]) + contribution(cols_prev, amp_other[2])
    sent_second = shifted(near_second, "occ", 1)
    first = jnp.concatenate([amp_halves[0], amp_other[0]], axis=0)
    second = jnp.concatenate([amp_other[0], amp_halves[0]], axis=0)
    own = contribution(b_cols, jnp.where(core == 0, first, second))
    sent = jnp.where(
        core == 0,
        jnp.concatenate([sent_first, sent_second], axis=1),
        jnp.concatenate([sent_second, sent_first], axis=1),
    )
    return own + sent


def solution(mesh):
    return jax.shard_map(
        per_device,
        mesh=mesh,
        in_specs=(P("aux", "occ"), P("aux", "occ"), P(), P(), P()),
        out_specs=P("aux", "occ"),
        check_vma=False,
    )
```

```python
import jax
import jax.numpy as jnp
from jax import lax
from jax.sharding import PartitionSpec as P

spin_scale = 1.3


def shifted(value, axis, by):
    size = lax.axis_size(axis)
    return lax.ppermute(value, axis, [(i, (i + by) % size) for i in range(size)])


def aux_pairs(size, step_core, step_chip):
    pairs = []
    for i in range(size):
        chip, core = divmod(i, 2)
        chips = size // 2
        pairs.append((i, ((chip + step_chip) % chips) * 2 + (core + step_core) % 2))
    return pairs


def partial_integrals(left_block, right_block):
    return lax.dot_general(
        left_block, right_block, (((0,), (0,)), ((), ())), preferred_element_type=jnp.float32
    )


def contribution(right_block, amplitude):
    return lax.dot_general(
        right_block, amplitude, (((1,), (1,)), ((), ())), preferred_element_type=jnp.float32
    )


def per_device(b_rows, b_cols, eps_occ, eps_va, eps_vb):
    per_block = b_rows.shape[1] // eps_va.shape[0]
    cycle_size = lax.axis_size("occ")
    position = lax.axis_index("occ")
    aux_size = lax.axis_size("aux")
    aux_pos = lax.axis_index("aux")
    core = aux_pos % 2
    chips = aux_size // 2
    rows = b_rows.shape[1]
    half = rows // 2

    def energy(offset, virt_energy):
        which = (position + offset) % cycle_size
        occ_energy = lax.dynamic_slice_in_dim(eps_occ, which * per_block, per_block)
        return (virt_energy[None, :] - occ_energy[:, None]).reshape(-1)

    def core_reduce(partials):
        stack = jnp.stack(partials)
        give = lax.dynamic_slice_in_dim(stack, (1 - core) * half, half, 1)
        keep = lax.dynamic_slice_in_dim(stack, core * half, half, 1)
        return keep + lax.ppermute(give, "aux", aux_pairs(aux_size, 1, 0))

    chip = aux_pos // 2
    piece = -(-half // chips)
    piece = -(-piece // 8) * 8

    def chip_reduce(summed):
        padded = jnp.pad(summed, ((0, 0), (0, piece * chips - half), (0, 0)))
        parts = padded.reshape(padded.shape[0], chips, piece, padded.shape[2])
        mine = lax.dynamic_index_in_dim(parts, chip, 1, keepdims=False)
        for d in range(1, chips):
            give = lax.dynamic_index_in_dim(parts, (chip + d) % chips, 1, keepdims=False)
            mine = mine + lax.ppermute(give, "aux", aux_pairs(aux_size, 0, d))
        return mine

    def chip_gather(mine):
        whole = jnp.zeros((mine.shape[0], chips, piece, mine.shape[2]), mine.dtype)
        whole = lax.dynamic_update_index_in_dim(whole, mine, chip, 1)
        for d in range(1, chips):
            got = lax.ppermute(mine, "aux", aux_pairs(aux_size, 0, d))
            whole = lax.dynamic_update_index_in_dim(whole, got, (chip - d) % chips, 1)
        return whole.reshape(mine.shape[0], chips * piece, mine.shape[2])[:, :half]

    def amplitude_part(summed, row_shift):
        row_energy = lax.dynamic_slice_in_dim(energy(row_shift, eps_va), core * half, half, 0)
        row_energy = jnp.pad(row_energy, (0, piece * chips - half), constant_values=1.0)
        row_energy = lax.dynamic_slice_in_dim(row_energy, chip * piece, piece, 0)
        col_energy = energy(0, eps_vb)
        return (spin_scale * summed / (row_energy[:, None] + col_energy[None, :])).astype(jnp.bfloat16)

    def chip_exchange(summed):
        others = [lax.ppermute(summed, "aux", aux_pairs(aux_size, 0, d)) for d in range(1, chips)]
        for other in others:
            summed = summed + other
        return summed

    def amplitude_half(summed, row_shift, col_shift):
        row_energy = lax.dynamic_slice_in_dim(energy(row_shift, eps_va), core * half, half, 0)
        col_energy = energy(col_shift, eps_vb)
        return (spin_scale * summed / (row_energy[:, None] + col_energy[None, :])).astype(jnp.bfloat16)

    cols_prev = shifted(b_cols, "occ", 1)
    rows_next = shifted(b_rows, "occ", -1)
    early = chip_reduce(core_reduce([partial_integrals(b_rows, b_cols), partial_integrals(rows_next, b_cols)]))
    early_amps = chip_gather(jnp.stack([amplitude_part(early[0], 0), amplitude_part(early[1], 1)]))
    late = chip_exchange(core_reduce([partial_integrals(rows_next, cols_prev)]))
    amp_halves = jnp.concatenate([early_amps, amplitude_half(late[0], 1, -1)[None]])
    sent_first = shifted(contribution(b_cols, amp_halves[1]) + contribution(cols_prev, amp_halves[2]), "occ", 1)
    amp_other = lax.ppermute(amp_halves, "aux", aux_pairs(aux_size, 1, 0))
    sent_second = shifted(contribution(b_cols, amp_other[1]) + contribution(cols_prev, amp_other[2]), "occ", 1)
    first = jnp.concatenate([amp_halves[0], amp_other[0]], axis=0)
    second = jnp.concatenate([amp_other[0], amp_halves[0]], axis=0)
    own = contribution(b_cols, jnp.where(core == 0, first, second))
    sent = jnp.where(
        core == 0,
        jnp.concatenate([sent_first, sent_second], axis=1),
        jnp.concatenate([sent_second, sent_first], axis=1),
    )
    return own + sent


def solution(mesh):
    return jax.shard_map(
        per_device,
        mesh=mesh,
        in_specs=(P("aux", "occ"), P("aux", "occ"), P(), P(), P()),
        out_specs=P("aux", "occ"),
        check_vma=False,
    )
```

```python
import jax
import jax.numpy as jnp
from jax import lax
from jax.sharding import PartitionSpec as P

spin_scale = 1.3


def shifted(value, axis, by):
    size = lax.axis_size(axis)
    return lax.ppermute(value, axis, [(i, (i + by) % size) for i in range(size)])


def aux_pairs(size, step_core, step_chip):
    pairs = []
    for i in range(size):
        chip, core = divmod(i, 2)
        chips = size // 2
        pairs.append((i, ((chip + step_chip) % chips) * 2 + (core + step_core) % 2))
    return pairs


def partial_integrals(left_block, right_block):
    return lax.dot_general(
        left_block, right_block, (((0,), (0,)), ((), ())), preferred_element_type=jnp.float32
    )


def contribution(right_block, amplitude):
    return lax.dot_general(
        right_block, amplitude, (((1,), (1,)), ((), ())), preferred_element_type=jnp.float32
    )


def per_device(b_rows, b_cols, eps_occ, eps_va, eps_vb):
    per_block = b_rows.shape[1] // eps_va.shape[0]
    cycle_size = lax.axis_size("occ")
    position = lax.axis_index("occ")
    aux_size = lax.axis_size("aux")
    aux_pos = lax.axis_index("aux")
    core = aux_pos % 2
    chips = aux_size // 2
    rows = b_rows.shape[1]
    half = rows // 2

    def energy(offset, virt_energy):
        which = (position + offset) % cycle_size
        occ_energy = lax.dynamic_slice_in_dim(eps_occ, which * per_block, per_block)
        return (virt_energy[None, :] - occ_energy[:, None]).reshape(-1)

    def core_reduce(partials):
        stack = jnp.stack(partials)
        give = lax.dynamic_slice_in_dim(stack, (1 - core) * half, half, 1)
        keep = lax.dynamic_slice_in_dim(stack, core * half, half, 1)
        return keep + lax.ppermute(give, "aux", aux_pairs(aux_size, 1, 0))

    def chip_reduce(summed):
        others = [lax.ppermute(summed, "aux", aux_pairs(aux_size, 0, d)) for d in range(1, chips)]
        for other in others:
            summed = summed + other
        return summed

    def amplitude_half(summed, row_shift, col_shift):
        row_energy = lax.dynamic_slice_in_dim(energy(row_shift, eps_va), core * half, half, 0)
        col_energy = energy(col_shift, eps_vb)
        return (spin_scale * summed / (row_energy[:, None] + col_energy[None, :])).astype(jnp.bfloat16)

    cols_prev = shifted(b_cols, "occ", 1)
    rows_next = shifted(b_rows, "occ", -1)
    early = chip_reduce(core_reduce([partial_integrals(b_rows, b_cols), partial_integrals(rows_next, b_cols)]))
    late = chip_reduce(core_reduce([partial_integrals(rows_next, cols_prev)]))
    amp_halves = jnp.stack([
        amplitude_half(early[0], 0, 0), amplitude_half(early[1], 1, 0), amplitude_half(late[0], 1, -1)
    ])
    near_first = contribution(b_cols, amp_halves[1]) + contribution(cols_prev, amp_halves[2])
    sent_first = shifted(near_first, "occ", 1)
    amp_other = lax.ppermute(amp_halves, "aux", aux_pairs(aux_size, 1, 0))
    near_second = contribution(b_cols, amp_other[1]) + contribution(cols_prev, amp_other[2])
    sent_second = shifted(near_second, "occ", 1)
    first = jnp.concatenate([amp_halves[0], amp_other[0]], axis=0)
    second = jnp.concatenate([amp_other[0], amp_halves[0]], axis=0)
    own = contribution(b_cols, jnp.where(core == 0, first, second))
    mine_at = core * half
    other_at = (1 - core) * half
    out = lax.dynamic_update_slice_in_dim(
        own, lax.dynamic_slice_in_dim(own, mine_at, half, 1) + sent_first, mine_at, 1)
    return lax.dynamic_update_slice_in_dim(
        out, lax.dynamic_slice_in_dim(own, other_at, half, 1) + sent_second, other_at, 1)


def solution(mesh):
    return jax.shard_map(
        per_device,
        mesh=mesh,
        in_specs=(P("aux", "occ"), P("aux", "occ"), P(), P(), P()),
        out_specs=P("aux", "occ"),
        check_vma=False,
    )
```
